32 devices in a mesh: gx: 2 (over core), gy: 2 (over x), gz: 8 (over z, y).
Axes of the slice: x: 2, y: 2, z: 4, core: 2. Of those that a mesh axis runs over, the one named last changes fastest.
Arguments:
- charges: bfloat16 [32, 48, 2048], P('gx', 'gy', 'gz'), may hold values from -6 to 6
- kernel_fine: bfloat16 [9, 9, 9], replicated, may hold values from -0.21875 to 0.21875
- kernel_mid: bfloat16 [9, 9, 9], replicated, may hold values from -0.21875 to 0.21875
- gauss_width: float32 [8], replicated, may hold values from 1 to 64
- gauss_weight: float32 [8], replicated, may hold values from 0.25 to 2
Outputs:
- potential: float32 [32, 48, 2048], P('gx', 'gy', 'gz')
The draws below stay inside these ranges and needn't reach their ends.
All inputs are finite; a program needn't handle non-finite values.
Results may differ from the reference program's by a relative error of at most 0.002.
Values may be sent and summed in bfloat16 or wider, within the bound.
No kernel may reach another device: no remote copies, remote signals or barrier semaphores. Data moves between devices by JAX's collectives and lax.ppermute only.
A program may use at most 384 MiB of HBM per device.

```python
import math
import jax
import jax.numpy as jnp
from jax import lax

M = 16
GAUSS = 8
NX = 32
NY = 48
NZ = 128
NX2 = 8
NY2 = 12
NZ2 = 32


def draw_gauss_width(key, part):
    offsets = jax.random.uniform(key, (GAUSS,), jnp.float32)
    levels = (jnp.arange(GAUSS, dtype=jnp.float32) + offsets) / GAUSS
    top = math.log(2.0 * NZ2)
    return jnp.clip(jnp.exp(levels * top), 1.0, 2.0 * NZ2).astype(jnp.float32)


def level_of(rng, shape, split, low, top_value):
    def one(axis_at, blocks):
        draws = jax.random.uniform(jax.random.fold_in(jax.random.fold_in(rng, 6), axis_at), (blocks,), jnp.float32, low / len(split), top_value / len(split))
        return jnp.repeat(jnp.exp(draws), shape[axis_at] // blocks).reshape((-1,) + (1,) * (len(shape) - axis_at - 1))

    gain = one(*split[0])
    for cut in split[1:]:
        gain = gain * one(*cut)
    return gain


def scatter_about(rng, dims, deviation, limit, pieces=(), kind=jnp.bfloat16):
    entries = deviation * jax.random.normal(rng, dims, jnp.float32)
    if pieces:
        entries = entries * level_of(rng, dims, pieces, -0.22, 0.18)
    return jnp.clip(entries, -limit, limit).astype(kind)


def setup_inputs(seed: int = 0) -> dict:
    splits = jax.random.split(jax.random.key(seed), 6)
    charges = scatter_about(splits[0], (NX, NY, NZ * M), 1.0, 6.0, ((0, 2), (1, 2), (2, 8)))
    kernel_fine = scatter_about(splits[1], (9, 9, 9), 729 ** -0.5, 0.21875)
    kernel_mid = scatter_about(splits[2], (9, 9, 9), 729 ** -0.5, 0.21875)
    gauss_width = draw_gauss_width(jax.random.fold_in(splits[5], 71), 0)
    gauss_weight = jnp.clip(jnp.exp(jax.random.uniform(splits[4], (GAUSS,), jnp.float32, math.log(0.25), math.log(2.0))), 0.25, 2.0)
    return {"charges": charges, "kernel_fine": kernel_fine, "kernel_mid": kernel_mid, "gauss_width": gauss_width, "gauss_weight": gauss_weight}


def stencil(offset):
    value = jnp.zeros(offset.shape, jnp.float32)
    value = jnp.where(jnp.abs(offset) == 1, 9.0 / 16.0, value)
    value = jnp.where(offset == 0, 1.0, value)
    value = jnp.where(jnp.abs(offset) == 3, -1.0 / 16.0, value)
    return value

def restriction(count):
    rows = jnp.arange(count // 2, dtype=jnp.int32)[:, None]
    cols = jnp.arange(count, dtype=jnp.int32)[None, :]
    return stencil(cols - 2 * rows)

def restrict_all(field):
    highest = lax.Precision.HIGHEST
    field = jnp.einsum('ia,abcm->ibcm', restriction(field.shape[0]), field, precision=highest)
    field = jnp.einsum('jb,ibcm->ijcm', restriction(field.shape[1]), field, precision=highest)
    field = jnp.einsum('kc,ijcm->ijkm', restriction(field.shape[2]), field, precision=highest)
    return field

def prolong_all(field):
    highest = lax.Precision.HIGHEST
    field = jnp.einsum('ai,abcm->ibcm', restriction(2 * field.shape[0]), field, precision=highest)
    field = jnp.einsum('bj,ibcm->ijcm', restriction(2 * field.shape[1]), field, precision=highest)
    field = jnp.einsum('ck,ijcm->ijkm', restriction(2 * field.shape[2]), field, precision=highest)
    return field

def correlate(field, kernel):
    source = jnp.transpose(field.astype(jnp.float32), (3, 0, 1, 2))[:, None]
    weights = kernel.astype(jnp.float32)[None, None]
    result = lax.conv_general_dilated(source, weights, (1, 1, 1), [(4, 4), (4, 4), (4, 4)], dimension_numbers=('NCDHW', 'OIDHW', 'NCDHW'), precision=lax.Precision.HIGHEST)
    return jnp.transpose(result[:, 0], (1, 2, 3, 0))

def gaussian(count, gauss_width):
    spots = jnp.arange(count, dtype=jnp.int32)
    spread = (spots[:, None] - spots[None, :]).astype(jnp.float32)
    width = gauss_width[:, None, None]
    return jnp.exp(-jnp.square(spread[None] / width)) / jnp.sqrt(width)

def reference(charges, kernel_fine, kernel_mid, gauss_width, gauss_weight):
    highest = lax.Precision.HIGHEST
    field = charges.reshape(NX, NY, NZ, M)
    short_fine = correlate(field, kernel_fine)
    q_mid = restrict_all(field.astype(jnp.float32)).astype(jnp.bfloat16)
    short_mid = correlate(q_mid, kernel_mid)
    q_top = restrict_all(q_mid.astype(jnp.float32))
    table_x = gaussian(NX2, gauss_width) * gauss_weight[:, None, None]
    section = jnp.einsum('gia,abcm->gibcm', table_x, q_top, precision=highest)
    section = jnp.einsum('gjb,gibcm->gijcm', gaussian(NY2, gauss_width), section, precision=highest)
    section = jnp.einsum('gkc,gijcm->gijkm', gaussian(NZ2, gauss_width), section, precision=highest)
    phi_top = lax.optimization_barrier(jnp.sum(section, axis=0))
    phi_mid = short_mid + prolong_all(phi_top)
    potential = short_fine + prolong_all(phi_mid)
    return potential.reshape(NX, NY, NZ * M)
```

```python
import jax
import jax.numpy as jnp
from jax import lax
from jax.sharding import PartitionSpec as P

M = 16


def padded_2(cells, sides, width):
    for axis, dim in sides:
        count = lax.axis_size(axis)
        ends = count - 1
        head = lax.slice_in_dim(cells, 0, width, axis=dim)
        tail = lax.slice_in_dim(cells, cells.shape[dim] - width, cells.shape[dim], axis=dim)
        cells = jnp.concatenate(
            [
                lax.ppermute(tail, axis, [(i, (i + 1) % count) for i in range(ends)]),
                cells,
                lax.ppermute(head, axis, [((i + 1) % count, i) for i in range(ends)]),
            ],
            axis=dim,
        )
    return cells


def stencil(offset):
    value = jnp.zeros(offset.shape, jnp.float32)
    value = jnp.where(jnp.abs(offset) == 1, 9.0 / 16.0, value)
    value = jnp.where(offset == 0, 1.0, value)
    value = jnp.where(jnp.abs(offset) == 3, -1.0 / 16.0, value)
    return value


def restrict_band(rows, cols, margin):
    row_ids = jnp.arange(rows, dtype=jnp.int32)[:, None]
    col_ids = jnp.arange(cols, dtype=jnp.int32)[None, :]
    return stencil(col_ids - margin - 2 * row_ids)


def prolong_band(rows, cols):
    row_ids = jnp.arange(rows, dtype=jnp.int32)[:, None]
    col_ids = jnp.arange(cols, dtype=jnp.int32)[None, :]
    return stencil(row_ids - 2 * col_ids + 4)


def restrict_padded(padded, sizes, margin):
    highest = lax.Precision.HIGHEST
    band_x = restrict_band(sizes[0], padded.shape[0], margin).astype(jnp.bfloat16)
    band_y = restrict_band(sizes[1], padded.shape[1], margin)
    band_z = restrict_band(sizes[2], padded.shape[2], margin)
    field = jnp.einsum("ia,abcm->ibcm", band_x, padded, preferred_element_type=jnp.float32)
    field = jnp.einsum("jb,ibcm->ijcm", band_y, field, precision=highest)
    field = jnp.einsum("kc,ijcm->ijkm", band_z, field, precision=highest)
    return field


def prolong_ext(field, sizes):
    highest = lax.Precision.HIGHEST
    field = jnp.einsum(
        "ia,abcm->ibcm", prolong_band(sizes[0], field.shape[0]), field, precision=highest
    )
    field = jnp.einsum(
        "jb,ibcm->ijcm", prolong_band(sizes[1], field.shape[1]), field, precision=highest
    )
    field = jnp.einsum(
        "kc,ijcm->ijkm", prolong_band(sizes[2], field.shape[2]), field, precision=highest
    )
    return field


def correlate(padded, kernel, out_sizes):
    reach = jnp.arange(9, dtype=jnp.int32)[:, None, None]
    lag_y = (
        jnp.arange(padded.shape[1], dtype=jnp.int32)[:, None]
        - jnp.arange(out_sizes[1], dtype=jnp.int32)[None, :]
    )
    lag_z = (
        jnp.arange(padded.shape[2], dtype=jnp.int32)[:, None]
        - jnp.arange(out_sizes[2], dtype=jnp.int32)[None, :]
    )
    pick_y = (lag_y[None] == reach).astype(jnp.bfloat16)
    pick_z = (lag_z[None] == reach).astype(jnp.bfloat16)
    total = jnp.zeros((out_sizes[0], out_sizes[1], out_sizes[2], padded.shape[3]), jnp.float32)
    for offset in range(9):
        table = jnp.einsum(
            "bc,bpy,cqz->pqyz", kernel[offset], pick_y, pick_z, preferred_element_type=jnp.float32
        ).astype(jnp.bfloat16)
        total = total + jnp.einsum(
            "xpqm,pqyz->xyzm",
            padded[offset : offset + out_sizes[0]],
            table,
            preferred_element_type=jnp.float32,
        )
    return total


def gaussian_table(first_row, rows, cols, whole, gauss_width):
    row_pos = first_row + jnp.arange(rows, dtype=jnp.int32)
    col_pos = jnp.arange(cols, dtype=jnp.int32)
    spread = (row_pos[:, None] - col_pos[None, :]).astype(jnp.float32)
    width = gauss_width[:, None, None]
    table = jnp.exp(-jnp.square(spread[None] / width)) / jnp.sqrt(width)
    inside = (row_pos >= 0) & (row_pos < whole)
    return jnp.where(inside[None, :, None], table, 0.0)


def inside_mask(position, count, local, rim):
    spots = position * local - rim + jnp.arange(local + 2 * rim, dtype=jnp.int32)
    return ((spots >= 0) & (spots < local * count)).astype(jnp.float32)


def per_device(charges, kernel_fine, kernel_mid, gauss_width, gauss_weight):
    highest = lax.Precision.HIGHEST
    size_x, size_y, flat = charges.shape
    members = M
    size_z = flat // members
    field = charges.reshape(size_x, size_y, size_z, members)
    padded = padded_2(field, (("gx", 0), ("gy", 1), ("gz", 2)), 4)
    short_fine = correlate(padded, kernel_fine, (size_x, size_y, size_z))
    mid_sizes = (size_x // 2, size_y // 2, size_z // 2)
    q_mid = restrict_padded(padded, mid_sizes, 4).astype(jnp.bfloat16)
    mid_padded = padded_2(q_mid, (("gx", 0), ("gy", 1), ("gz", 2)), 6)
    short_mid = correlate(
        mid_padded, kernel_mid, (mid_sizes[0] + 4, mid_sizes[1] + 4, mid_sizes[2] + 4)
    )
    top_x, top_y, top_z = (size_x // 4, size_y // 4, size_z // 4)
    q_top = restrict_padded(mid_padded, (top_x, top_y, top_z), 6)
    count_x = lax.axis_size("gx")
    count_y = lax.axis_size("gy")
    count_z = lax.axis_size("gz")
    index_x = lax.axis_index("gx")
    index_y = lax.axis_index("gy")
    index_z = lax.axis_index("gz")
    whole_x = top_x * count_x
    whole_y = top_y * count_y
    whole_z = top_z * count_z
    first_x = index_x * top_x - 3
    first_y = index_y * top_y - 3
    first_z = index_z * top_z - 3
    scaled = gauss_weight[:, None, None]
    flat = q_top.reshape(-1)
    block = flat.shape[0]
    rows = -(-block // 1024) * 8
    chunk = jnp.pad(flat, (0, rows * 128 - block)).reshape(rows, 128)
    gathered = lax.all_gather(chunk, ("gx", "gy", "gz"), axis=0, tiled=True)
    gathered = gathered.reshape(count_x, count_y, count_z, rows * 128)[..., :block]
    gathered = gathered.reshape(count_x, count_y, count_z, top_x, top_y, top_z, members)
    q_full = gathered.transpose(0, 3, 1, 4, 2, 5, 6).reshape(whole_x, whole_y, whole_z, members)
    table_x = gaussian_table(first_x, top_x + 6, whole_x, whole_x, gauss_width) * scaled
    table_y = gaussian_table(first_y, top_y + 6, whole_y, whole_y, gauss_width)
    table_z = gaussian_table(first_z, top_z + 6, whole_z, whole_z, gauss_width)
    section = jnp.einsum("gkc,abcm->gabkm", table_z, q_full, precision=highest)
    section = jnp.einsum("gjb,gabkm->gajkm", table_y, section, precision=highest)
    phi_top = jnp.einsum("gia,gajkm->ijkm", table_x, section, precision=highest)
    ext_sizes = (mid_sizes[0] + 4, mid_sizes[1] + 4, mid_sizes[2] + 4)
    phi_mid = short_mid + prolong_ext(phi_top, ext_sizes)
    mask_x = inside_mask(index_x, count_x, mid_sizes[0], 2)
    mask_y = inside_mask(index_y, count_y, mid_sizes[1], 2)
    mask_z = inside_mask(index_z, count_z, mid_sizes[2], 2)
    phi_mid = (
        phi_mid
        * mask_x[:, None, None, None]
        * mask_y[None, :, None, None]
        * mask_z[None, None, :, None]
    )
    potential = short_fine + prolong_ext(phi_mid, (size_x, size_y, size_z))
    return potential.reshape(size_x, size_y, size_z * members)


def solution(mesh):
    placed = (P("gx", "gy", "gz"), P(), P(), P(), P())
    return jax.shard_map(
        per_device, mesh=mesh, in_specs=placed, out_specs=P("gx", "gy", "gz"), check_vma=False
    )
```

```python
import jax
import jax.numpy as jnp
from jax import lax
from jax.sharding import PartitionSpec as P

M = 16


def padded_2(cells, sides, width):
    for axis, dim in sides:
        count = lax.axis_size(axis)
        ends = count - 1
        head = lax.slice_in_dim(cells, 0, width, axis=dim)
        tail = lax.slice_in_dim(cells, cells.shape[dim] - width, cells.shape[dim], axis=dim)
        cells = jnp.concatenate(
            [
                lax.ppermute(tail, axis, [(i, (i + 1) % count) for i in range(ends)]),
                cells,
                lax.ppermute(head, axis, [((i + 1) % count, i) for i in range(ends)]),
            ],
            axis=dim,
        )
    return cells


def stencil(offset):
    value = jnp.zeros(offset.shape, jnp.float32)
    value = jnp.where(jnp.abs(offset) == 1, 9.0 / 16.0, value)
    value = jnp.where(offset == 0, 1.0, value)
    value = jnp.where(jnp.abs(offset) == 3, -1.0 / 16.0, value)
    return value


def restrict_band(rows, cols, margin):
    row_ids = jnp.arange(rows, dtype=jnp.int32)[:, None]
    col_ids = jnp.arange(cols, dtype=jnp.int32)[None, :]
    return stencil(col_ids - margin - 2 * row_ids)


def prolong_band(rows, cols):
    row_ids = jnp.arange(rows, dtype=jnp.int32)[:, None]
    col_ids = jnp.arange(cols, dtype=jnp.int32)[None, :]
    return stencil(row_ids - 2 * col_ids + 4)


def restrict_padded(padded, sizes, margin):
    highest = lax.Precision.HIGHEST
    band_x = restrict_band(sizes[0], padded.shape[0], margin).astype(jnp.bfloat16)
    band_y = restrict_band(sizes[1], padded.shape[1], margin)
    band_z = restrict_band(sizes[2], padded.shape[2], margin)
    field = jnp.einsum("ia,abcm->ibcm", band_x, padded, preferred_element_type=jnp.float32)
    field = jnp.einsum("jb,ibcm->ijcm", band_y, field, precision=highest)
    field = jnp.einsum("kc,ijcm->ijkm", band_z, field, precision=highest)
    return field


def prolong_ext(field, sizes):
    highest = lax.Precision.HIGHEST
    field = jnp.einsum(
        "ia,abcm->ibcm", prolong_band(sizes[0], field.shape[0]), field, precision=highest
    )
    field = jnp.einsum(
        "jb,ibcm->ijcm", prolong_band(sizes[1], field.shape[1]), field, precision=highest
    )
    field = jnp.einsum(
        "kc,ijcm->ijkm", prolong_band(sizes[2], field.shape[2]), field, precision=highest
    )
    return field


def correlate(padded, kernel, out_sizes):
    reach = jnp.arange(9, dtype=jnp.int32)[:, None, None]
    lag_y = (
        jnp.arange(padded.shape[1], dtype=jnp.int32)[:, None]
        - jnp.arange(out_sizes[1], dtype=jnp.int32)[None, :]
    )
    lag_z = (
        jnp.arange(padded.shape[2], dtype=jnp.int32)[:, None]
        - jnp.arange(out_sizes[2], dtype=jnp.int32)[None, :]
    )
    pick_y = (lag_y[None] == reach).astype(jnp.bfloat16)
    pick_z = (lag_z[None] == reach).astype(jnp.bfloat16)
    total = jnp.zeros((out_sizes[0], out_sizes[1], out_sizes[2], padded.shape[3]), jnp.float32)
    for offset in range(9):
        table = jnp.einsum(
            "bc,bpy,cqz->pqyz", kernel[offset], pick_y, pick_z, preferred_element_type=jnp.float32
        ).astype(jnp.bfloat16)
        total = total + jnp.einsum(
            "xpqm,pqyz->xyzm",
            padded[offset : offset + out_sizes[0]],
            table,
            preferred_element_type=jnp.float32,
        )
    return total


def gaussian_table(first_row, rows, cols, whole, gauss_width):
    row_pos = first_row + jnp.arange(rows, dtype=jnp.int32)
    col_pos = jnp.arange(cols, dtype=jnp.int32)
    spread = (row_pos[:, None] - col_pos[None, :]).astype(jnp.float32)
    width = gauss_width[:, None, None]
    table = jnp.exp(-jnp.square(spread[None] / width)) / jnp.sqrt(width)
    inside = (row_pos >= 0) & (row_pos < whole)
    return jnp.where(inside[None, :, None], table, 0.0)


def inside_mask(position, count, local, rim):
    spots = position * local - rim + jnp.arange(local + 2 * rim, dtype=jnp.int32)
    return ((spots >= 0) & (spots < local * count)).astype(jnp.float32)


def per_device(charges, kernel_fine, kernel_mid, gauss_width, gauss_weight):
    highest = lax.Precision.HIGHEST
    size_x, size_y, flat = charges.shape
    members = M
    size_z = flat // members
    field = charges.reshape(size_x, size_y, size_z, members)
    padded = padded_2(field, (("gx", 0), ("gy", 1), ("gz", 2)), 4)
    short_fine = correlate(padded, kernel_fine, (size_x, size_y, size_z))
    mid_sizes = (size_x // 2, size_y // 2, size_z // 2)
    q_mid = restrict_padded(padded, mid_sizes, 4).astype(jnp.bfloat16)
    mid_padded = padded_2(q_mid, (("gx", 0), ("gy", 1), ("gz", 2)), 6)
    short_mid = correlate(
        mid_padded, kernel_mid, (mid_sizes[0] + 4, mid_sizes[1] + 4, mid_sizes[2] + 4)
    )
    top_x, top_y, top_z = (size_x // 4, size_y // 4, size_z // 4)
    q_top = restrict_padded(mid_padded, (top_x, top_y, top_z), 6)
    count_x = lax.axis_size("gx")
    count_y = lax.axis_size("gy")
    count_z = lax.axis_size("gz")
    index_x = lax.axis_index("gx")
    index_y = lax.axis_index("gy")
    index_z = lax.axis_index("gz")
    whole_x = top_x * count_x
    whole_y = top_y * count_y
    whole_z = top_z * count_z
    first_x = index_x * top_x - 3
    first_y = index_y * top_y - 3
    first_z = index_z * top_z - 3
    scaled = gauss_weight[:, None, None]
    flat = q_top.reshape(-1)
    block = flat.shape[0]
    rows = -(-block // 1024) * 8
    chunk = jnp.pad(flat, (0, rows * 128 - block)).reshape(rows, 128)
    full = jnp.zeros((count_x * count_y * count_z * rows, 128), jnp.float32)
    me = (index_x * count_y + index_y) * count_z + index_z
    gathered = lax.psum(lax.dynamic_update_slice(full, chunk, (me * rows, 0)), ("gx", "gy", "gz"))
    gathered = gathered.reshape(count_x, count_y, count_z, rows * 128)[..., :block]
    gathered = gathered.reshape(count_x, count_y, count_z, top_x, top_y, top_z, members)
    q_full = gathered.transpose(0, 3, 1, 4, 2, 5, 6).reshape(whole_x, whole_y, whole_z, members)
    table_x = gaussian_table(first_x, top_x + 6, whole_x, whole_x, gauss_width) * scaled
    table_y = gaussian_table(first_y, top_y + 6, whole_y, whole_y, gauss_width)
    table_z = gaussian_table(first_z, top_z + 6, whole_z, whole_z, gauss_width)
    section = jnp.einsum("gkc,abcm->gabkm", table_z, q_full, precision=highest)
    section = jnp.einsum("gjb,gabkm->gajkm", table_y, section, precision=highest)
    phi_top = jnp.einsum("gia,gajkm->ijkm", table_x, section, precision=highest)
    ext_sizes = (mid_sizes[0] + 4, mid_sizes[1] + 4, mid_sizes[2] + 4)
    phi_mid = short_mid + prolong_ext(phi_top, ext_sizes)
    mask_x = inside_mask(index_x, count_x, mid_sizes[0], 2)
    mask_y = inside_mask(index_y, count_y, mid_sizes[1], 2)
    mask_z = inside_mask(index_z, count_z, mid_sizes[2], 2)
    phi_mid = (
        phi_mid
        * mask_x[:, None, None, None]
        * mask_y[None, :, None, None]
        * mask_z[None, None, :, None]
    )
    potential = short_fine + prolong_ext(phi_mid, (size_x, size_y, size_z))
    return potential.reshape(size_x, size_y, size_z * members)


def solution(mesh):
    placed = (P("gx", "gy", "gz"), P(), P(), P(), P())
    return jax.shard_map(
        per_device, mesh=mesh, in_specs=placed, out_specs=P("gx", "gy", "gz"), check_vma=False
    )
```

```python
import jax
import jax.numpy as jnp
from jax import lax
from jax.sharding import PartitionSpec as P

M = 16


def padded_2(cells, sides, width):
    for axis, dim in sides:
        count = lax.axis_size(axis)
        ends = count - 1
        head = lax.slice_in_dim(cells, 0, width, axis=dim)
        tail = lax.slice_in_dim(cells, cells.shape[dim] - width, cells.shape[dim], axis=dim)
        cells = jnp.concatenate(
            [
                lax.ppermute(tail, axis, [(i, (i + 1) % count) for i in range(ends)]),
                cells,
                lax.ppermute(head, axis, [((i + 1) % count, i) for i in range(ends)]),
            ],
            axis=dim,
        )
    return cells


def stencil(offset):
    value = jnp.zeros(offset.shape, jnp.float32)
    value = jnp.where(jnp.abs(offset) == 1, 9.0 / 16.0, value)
    value = jnp.where(offset == 0, 1.0, value)
    value = jnp.where(jnp.abs(offset) == 3, -1.0 / 16.0, value)
    return value


def restrict_band(rows, cols, margin):
    row_ids = jnp.arange(rows, dtype=jnp.int32)[:, None]
    col_ids = jnp.arange(cols, dtype=jnp.int32)[None, :]
    return stencil(col_ids - margin - 2 * row_ids)


def prolong_band(rows, cols):
    row_ids = jnp.arange(rows, dtype=jnp.int32)[:, None]
    col_ids = jnp.arange(cols, dtype=jnp.int32)[None, :]
    return stencil(row_ids - 2 * col_ids + 4)


def restrict_padded(padded, sizes, margin):
    highest = lax.Precision.HIGHEST
    band_x = restrict_band(sizes[0], padded.shape[0], margin).astype(jnp.bfloat16)
    band_y = restrict_band(sizes[1], padded.shape[1], margin)
    band_z = restrict_band(sizes[2], padded.shape[2], margin)
    field = jnp.einsum("ia,abcm->ibcm", band_x, padded, preferred_element_type=jnp.float32)
    field = jnp.einsum("jb,ibcm->ijcm", band_y, field, precision=highest)
    field = jnp.einsum("kc,ijcm->ijkm", band_z, field, precision=highest)
    return field


def prolong_ext(field, sizes):
    highest = lax.Precision.HIGHEST
    field = jnp.einsum(
        "ia,abcm->ibcm", prolong_band(sizes[0], field.shape[0]), field, precision=highest
    )
    field = jnp.einsum(
        "jb,ibcm->ijcm", prolong_band(sizes[1], field.shape[1]), field, precision=highest
    )
    field = jnp.einsum(
        "kc,ijcm->ijkm", prolong_band(sizes[2], field.shape[2]), field, precision=highest
    )
    return field


def correlate(padded, kernel, out_sizes):
    reach = jnp.arange(9, dtype=jnp.int32)[:, None, None]
    lag_y = (
        jnp.arange(padded.shape[1], dtype=jnp.int32)[:, None]
        - jnp.arange(out_sizes[1], dtype=jnp.int32)[None, :]
    )
    lag_z = (
        jnp.arange(padded.shape[2], dtype=jnp.int32)[:, None]
        - jnp.arange(out_sizes[2], dtype=jnp.int32)[None, :]
    )
    pick_y = (lag_y[None] == reach).astype(jnp.bfloat16)
    pick_z = (lag_z[None] == reach).astype(jnp.bfloat16)
    total = jnp.zeros((out_sizes[0], out_sizes[1], out_sizes[2], padded.shape[3]), jnp.float32)
    for offset in range(9):
        table = jnp.einsum(
            "bc,bpy,cqz->pqyz", kernel[offset], pick_y, pick_z, preferred_element_type=jnp.float32
        ).astype(jnp.bfloat16)
        total = total + jnp.einsum(
            "xpqm,pqyz->xyzm",
            padded[offset : offset + out_sizes[0]],
            table,
            preferred_element_type=jnp.float32,
        )
    return total


def gaussian_table(first_row, rows, cols, whole, gauss_width):
    row_pos = first_row + jnp.arange(rows, dtype=jnp.int32)
    col_pos = jnp.arange(cols, dtype=jnp.int32)
    spread = (row_pos[:, None] - col_pos[None, :]).astype(jnp.float32)
    width = gauss_width[:, None, None]
    table = jnp.exp(-jnp.square(spread[None] / width)) / jnp.sqrt(width)
    inside = (row_pos >= 0) & (row_pos < whole)
    return jnp.where(inside[None, :, None], table, 0.0)


def xor_gather(block, axis):
    count = lax.axis_size(axis)
    if count & (count - 1):
        return lax.all_gather(block, axis, axis=0, tiled=False), False
    parts = block[None]
    step = 1
    while step < count:
        other = lax.ppermute(parts, axis, [(i, i ^ step) for i in range(count)])
        parts = jnp.concatenate([parts, other], axis=0)
        step *= 2
    return parts, True


def gaussian_cols(first_row, rows, index, count, local, whole, gauss_width, flipped):
    row_pos = first_row + jnp.arange(rows, dtype=jnp.int32)
    place = jnp.arange(count, dtype=jnp.int32)
    source = jnp.bitwise_xor(index, place) if flipped else place
    col_pos = (source[:, None] * local + jnp.arange(local, dtype=jnp.int32)[None, :]).reshape(-1)
    spread = (row_pos[:, None] - col_pos[None, :]).astype(jnp.float32)
    width = gauss_width[:, None, None]
    table = jnp.exp(-jnp.square(spread[None] / width)) / jnp.sqrt(width)
    inside = (row_pos >= 0) & (row_pos < whole)
    return jnp.where(inside[None, :, None], table, 0.0)


def inside_mask(position, count, local, rim):
    spots = position * local - rim + jnp.arange(local + 2 * rim, dtype=jnp.int32)
    return ((spots >= 0) & (spots < local * count)).astype(jnp.float32)


def per_device(charges, kernel_fine, kernel_mid, gauss_width, gauss_weight):
    highest = lax.Precision.HIGHEST
    size_x, size_y, flat = charges.shape
    members = M
    size_z = flat // members
    field = charges.reshape(size_x, size_y, size_z, members)
    padded = padded_2(field, (("gx", 0), ("gy", 1), ("gz", 2)), 4)
    short_fine = correlate(padded, kernel_fine, (size_x, size_y, size_z))
    mid_sizes = (size_x // 2, size_y // 2, size_z // 2)
    q_mid = restrict_padded(padded, mid_sizes, 4).astype(jnp.bfloat16)
    mid_padded = padded_2(q_mid, (("gx", 0), ("gy", 1), ("gz", 2)), 6)
    short_mid = correlate(
        mid_padded, kernel_mid, (mid_sizes[0] + 4, mid_sizes[1] + 4, mid_sizes[2] + 4)
    )
    top_x, top_y, top_z = (size_x // 4, size_y // 4, size_z // 4)
    q_top = restrict_padded(mid_padded, (top_x, top_y, top_z), 6)
    count_x = lax.axis_size("gx")
    count_y = lax.axis_size("gy")
    count_z = lax.axis_size("gz")
    index_x = lax.axis_index("gx")
    index_y = lax.axis_index("gy")
    index_z = lax.axis_index("gz")
    whole_x = top_x * count_x
    whole_y = top_y * count_y
    whole_z = top_z * count_z
    first_x = index_x * top_x - 3
    first_y = index_y * top_y - 3
    first_z = index_z * top_z - 3
    scaled = gauss_weight[:, None, None]
    flat = q_top.reshape(-1)
    block = flat.shape[0]
    lanes = -(-block // 128) * 128
    parts = jnp.pad(flat, (0, lanes - block)).reshape(lanes // 128, 128)
    parts, flip_z = xor_gather(parts, "gz")
    parts, flip_y = xor_gather(parts, "gy")
    parts, flip_x = xor_gather(parts, "gx")
    parts = parts.reshape(count_x, count_y, count_z, lanes)[..., :block]
    parts = parts.reshape(count_x, count_y, count_z, top_x, top_y, top_z, members)
    q_full = parts.transpose(0, 3, 1, 4, 2, 5, 6).reshape(whole_x, whole_y, whole_z, members)
    table_x = gaussian_cols(first_x, top_x + 6, index_x, count_x, top_x, whole_x, gauss_width, flip_x) * scaled
    table_y = gaussian_cols(first_y, top_y + 6, index_y, count_y, top_y, whole_y, gauss_width, flip_y)
    table_z = gaussian_cols(first_z, top_z + 6, index_z, count_z, top_z, whole_z, gauss_width, flip_z)
    section = jnp.einsum("gkc,abcm->gabkm", table_z, q_full, precision=highest)
    section = jnp.einsum("gjb,gabkm->gajkm", table_y, section, precision=highest)
    phi_top = jnp.einsum("gia,gajkm->ijkm", table_x, section, precision=highest)
    ext_sizes = (mid_sizes[0] + 4, mid_sizes[1] + 4, mid_sizes[2] + 4)
    phi_mid = short_mid + prolong_ext(phi_top, ext_sizes)
    mask_x = inside_mask(index_x, count_x, mid_sizes[0], 2)
    mask_y = inside_mask(index_y, count_y, mid_sizes[1], 2)
    mask_z = inside_mask(index_z, count_z, mid_sizes[2], 2)
    phi_mid = (
        phi_mid
        * mask_x[:, None, None, None]
        * mask_y[None, :, None, None]
        * mask_z[None, None, :, None]
    )
    potential = short_fine + prolong_ext(phi_mid, (size_x, size_y, size_z))
    return potential.reshape(size_x, size_y, size_z * members)


def solution(mesh):
    placed = (P("gx", "gy", "gz"), P(), P(), P(), P())
    return jax.shard_map(
        per_device, mesh=mesh, in_specs=placed, out_specs=P("gx", "gy", "gz"), check_vma=False
    )
```

```python
import jax
import jax.numpy as jnp
from jax import lax
from jax.sharding import PartitionSpec as P

M = 16


def padded_2(cells, sides, width):
    for axis, dim in sides:
        count = lax.axis_size(axis)
        ends = count - 1
        head = lax.slice_in_dim(cells, 0, width, axis=dim)
        tail = lax.slice_in_dim(cells, cells.shape[dim] - width, cells.shape[dim], axis=dim)
        cells = jnp.concatenate(
            [
                lax.ppermute(tail, axis, [(i, (i + 1) % count) for i in range(ends)]),
                cells,
                lax.ppermute(head, axis, [((i + 1) % count, i) for i in range(ends)]),
            ],
            axis=dim,
        )
    return cells


def stencil(offset):
    value = jnp.zeros(offset.shape, jnp.float32)
    value = jnp.where(jnp.abs(offset) == 1, 9.0 / 16.0, value)
    value = jnp.where(offset == 0, 1.0, value)
    value = jnp.where(jnp.abs(offset) == 3, -1.0 / 16.0, value)
    return value


def restrict_band(rows, cols, margin):
    row_ids = jnp.arange(rows, dtype=jnp.int32)[:, None]
    col_ids = jnp.arange(cols, dtype=jnp.int32)[None, :]
    return stencil(col_ids - margin - 2 * row_ids)


def prolong_band(rows, cols):
    row_ids = jnp.arange(rows, dtype=jnp.int32)[:, None]
    col_ids = jnp.arange(cols, dtype=jnp.int32)[None, :]
    return stencil(row_ids - 2 * col_ids + 4)


def restrict_padded(padded, sizes, margin):
    highest = lax.Precision.HIGHEST
    band_x = restrict_band(sizes[0], padded.shape[0], margin).astype(jnp.bfloat16)
    band_y = restrict_band(sizes[1], padded.shape[1], margin)
    band_z = restrict_band(sizes[2], padded.shape[2], margin)
    field = jnp.einsum("ia,abcm->ibcm", band_x, padded, preferred_element_type=jnp.float32)
    field = jnp.einsum("jb,ibcm->ijcm", band_y, field, precision=highest)
    field = jnp.einsum("kc,ijcm->ijkm", band_z, field, precision=highest)
    return field


def prolong_ext(field, sizes):
    highest = lax.Precision.HIGH
    field = jnp.einsum(
        "ia,abcm->ibcm", prolong_band(sizes[0], field.shape[0]), field, precision=highest
    )
    field = jnp.einsum(
        "jb,ibcm->ijcm", prolong_band(sizes[1], field.shape[1]), field, precision=highest
    )
    field = jnp.einsum(
        "kc,ijcm->ijkm", prolong_band(sizes[2], field.shape[2]), field, precision=highest
    )
    return field


def correlate(padded, kernel, out_sizes):
    reach = jnp.arange(9, dtype=jnp.int32)[:, None, None]
    lag_y = (
        jnp.arange(padded.shape[1], dtype=jnp.int32)[:, None]
        - jnp.arange(out_sizes[1], dtype=jnp.int32)[None, :]
    )
    lag_z = (
        jnp.arange(padded.shape[2], dtype=jnp.int32)[:, None]
        - jnp.arange(out_sizes[2], dtype=jnp.int32)[None, :]
    )
    pick_y = (lag_y[None] == reach).astype(jnp.bfloat16)
    pick_z = (lag_z[None] == reach).astype(jnp.bfloat16)
    tables = jnp.einsum(
        "abc,bpy,cqz->apqyz", kernel, pick_y, pick_z, preferred_element_type=jnp.float32
    ).astype(jnp.bfloat16)
    stacked = jnp.stack([padded[offset : offset + out_sizes[0]] for offset in range(9)], axis=0)
    return jnp.einsum("axpqm,apqyz->xyzm", stacked, tables, preferred_element_type=jnp.float32)


def gaussian_table(first_row, rows, cols, whole, gauss_width):
    row_pos = first_row + jnp.arange(rows, dtype=jnp.int32)
    col_pos = jnp.arange(cols, dtype=jnp.int32)
    spread = (row_pos[:, None] - col_pos[None, :]).astype(jnp.float32)
    width = gauss_width[:, None, None]
    table = jnp.exp(-jnp.square(spread[None] / width)) / jnp.sqrt(width)
    inside = (row_pos >= 0) & (row_pos < whole)
    return jnp.where(inside[None, :, None], table, 0.0)


def xor_gather(block, axis):
    count = lax.axis_size(axis)
    if count & (count - 1):
        return lax.all_gather(block, axis, axis=0, tiled=False), False
    parts = block[None]
    step = 1
    while step < count:
        other = lax.ppermute(parts, axis, [(i, i ^ step) for i in range(count)])
        parts = jnp.concatenate([parts, other], axis=0)
        step *= 2
    return parts, True


def gaussian_cols(first_row, rows, index, count, local, whole, gauss_width, flipped):
    row_pos = first_row + jnp.arange(rows, dtype=jnp.int32)
    place = jnp.arange(count, dtype=jnp.int32)
    source = jnp.bitwise_xor(index, place) if flipped else place
    col_pos = (source[:, None] * local + jnp.arange(local, dtype=jnp.int32)[None, :]).reshape(-1)
    spread = (row_pos[:, None] - col_pos[None, :]).astype(jnp.float32)
    width = gauss_width[:, None, None]
    table = jnp.exp(-jnp.square(spread[None] / width)) / jnp.sqrt(width)
    inside = (row_pos >= 0) & (row_pos < whole)
    return jnp.where(inside[None, :, None], table, 0.0)


def inside_mask(position, count, local, rim):
    spots = position * local - rim + jnp.arange(local + 2 * rim, dtype=jnp.int32)
    return ((spots >= 0) & (spots < local * count)).astype(jnp.float32)


def per_device(charges, kernel_fine, kernel_mid, gauss_width, gauss_weight):
    highest = lax.Precision.HIGHEST
    size_x, size_y, flat = charges.shape
    members = M
    size_z = flat // members
    field = charges.reshape(size_x, size_y, size_z, members)
    padded = padded_2(field, (("gx", 0), ("gy", 1), ("gz", 2)), 4)
    short_fine = correlate(padded, kernel_fine, (size_x, size_y, size_z))
    mid_sizes = (size_x // 2, size_y // 2, size_z // 2)
    q_mid = restrict_padded(padded, mid_sizes, 4).astype(jnp.bfloat16)
    mid_padded = padded_2(q_mid, (("gx", 0), ("gy", 1), ("gz", 2)), 6)
    short_mid = correlate(
        mid_padded, kernel_mid, (mid_sizes[0] + 4, mid_sizes[1] + 4, mid_sizes[2] + 4)
    )
    top_x, top_y, top_z = (size_x // 4, size_y // 4, size_z // 4)
    q_top = restrict_padded(mid_padded, (top_x, top_y, top_z), 6)
    count_x = lax.axis_size("gx")
    count_y = lax.axis_size("gy")
    count_z = lax.axis_size("gz")
    index_x = lax.axis_index("gx")
    index_y = lax.axis_index("gy")
    index_z = lax.axis_index("gz")
    whole_x = top_x * count_x
    whole_y = top_y * count_y
    whole_z = top_z * count_z
    first_x = index_x * top_x - 3
    first_y = index_y * top_y - 3
    first_z = index_z * top_z - 3
    scaled = gauss_weight[:, None, None]
    flat = q_top.reshape(-1)
    block = flat.shape[0]
    lanes = -(-block // 128) * 128
    parts = jnp.pad(flat, (0, lanes - block)).reshape(lanes // 128, 128)
    parts, flip_z = xor_gather(parts, "gz")
    parts, flip_y = xor_gather(parts, "gy")
    parts, flip_x = xor_gather(parts, "gx")
    parts = parts.reshape(count_x, count_y, count_z, lanes)[..., :block]
    parts = parts.reshape(count_x, count_y, count_z, top_x, top_y, top_z, members)
    q_full = parts.transpose(0, 3, 1, 4, 2, 5, 6).reshape(whole_x, whole_y, whole_z, members)
    table_x = gaussian_cols(first_x, top_x + 6, index_x, count_x, top_x, whole_x, gauss_width, flip_x) * scaled
    table_y = gaussian_cols(first_y, top_y + 6, index_y, count_y, top_y, whole_y, gauss_width, flip_y)
    table_z = gaussian_cols(first_z, top_z + 6, index_z, count_z, top_z, whole_z, gauss_width, flip_z)
    high = lax.Precision.HIGH
    section = jnp.einsum("gkc,abcm->gabkm", table_z, q_full, precision=high)
    section = jnp.einsum("gjb,gabkm->gajkm", table_y, section, precision=high)
    phi_top = jnp.einsum("gia,gajkm->ijkm", table_x, section, precision=high)
    ext_sizes = (mid_sizes[0] + 4, mid_sizes[1] + 4, mid_sizes[2] + 4)
    phi_mid = short_mid + prolong_ext(phi_top, ext_sizes)
    mask_x = inside_mask(index_x, count_x, mid_sizes[0], 2)
    mask_y = inside_mask(index_y, count_y, mid_sizes[1], 2)
    mask_z = inside_mask(index_z, count_z, mid_sizes[2], 2)
    phi_mid = (
        phi_mid
        * mask_x[:, None, None, None]
        * mask_y[None, :, None, None]
        * mask_z[None, None, :, None]
    )
    potential = short_fine + prolong_ext(phi_mid, (size_x, size_y, size_z))
    return potential.reshape(size_x, size_y, size_z * members)


def solution(mesh):
    placed = (P("gx", "gy", "gz"), P(), P(), P(), P())
    return jax.shard_map(
        per_device, mesh=mesh, in_specs=placed, out_specs=P("gx", "gy", "gz"), check_vma=False
    )
```

```python
import jax
import jax.numpy as jnp
from jax import lax
from jax.sharding import PartitionSpec as P

M = 16
FINE_TILE = 24
MID_TILE = 8


def padded_2(cells, sides, width):
    for axis, dim in sides:
        count = lax.axis_size(axis)
        ends = count - 1
        head = lax.slice_in_dim(cells, 0, width, axis=dim)
        tail = lax.slice_in_dim(cells, cells.shape[dim] - width, cells.shape[dim], axis=dim)
        cells = jnp.concatenate(
            [
                lax.ppermute(tail, axis, [(i, (i + 1) % count) for i in range(ends)]),
                cells,
                lax.ppermute(head, axis, [((i + 1) % count, i) for i in range(ends)]),
            ],
            axis=dim,
        )
    return cells


def stencil(offset):
    value = jnp.zeros(offset.shape, jnp.float32)
    value = jnp.where(jnp.abs(offset) == 1, 9.0 / 16.0, value)
    value = jnp.where(offset == 0, 1.0, value)
    value = jnp.where(jnp.abs(offset) == 3, -1.0 / 16.0, value)
    return value


def restrict_band(rows, cols, margin):
    row_ids = jnp.arange(rows, dtype=jnp.int32)[:, None]
    col_ids = jnp.arange(cols, dtype=jnp.int32)[None, :]
    return stencil(col_ids - margin - 2 * row_ids)


def prolong_band(rows, cols):
    row_ids = jnp.arange(rows, dtype=jnp.int32)[:, None]
    col_ids = jnp.arange(cols, dtype=jnp.int32)[None, :]
    return stencil(row_ids - 2 * col_ids + 4)


def restrict_padded(padded, sizes, margin):
    highest = lax.Precision.HIGHEST
    band_x = restrict_band(sizes[0], padded.shape[0], margin).astype(jnp.bfloat16)
    band_y = restrict_band(sizes[1], padded.shape[1], margin)
    band_z = restrict_band(sizes[2], padded.shape[2], margin)
    field = jnp.einsum("ia,abcm->ibcm", band_x, padded, preferred_element_type=jnp.float32)
    field = jnp.einsum("jb,ibcm->ijcm", band_y, field, precision=highest)
    field = jnp.einsum("kc,ijcm->ijkm", band_z, field, precision=highest)
    return field


def prolong_ext(field, sizes):
    highest = lax.Precision.HIGH
    field = jnp.einsum(
        "ia,abcm->ibcm", prolong_band(sizes[0], field.shape[0]), field, precision=highest
    )
    field = jnp.einsum(
        "jb,ibcm->ijcm", prolong_band(sizes[1], field.shape[1]), field, precision=highest
    )
    field = jnp.einsum(
        "kc,ijcm->ijkm", prolong_band(sizes[2], field.shape[2]), field, precision=highest
    )
    return field


def correlate(padded, kernel, out_sizes, tile):
    reach = jnp.arange(9, dtype=jnp.int32)[:, None, None]
    lag_y = (
        jnp.arange(tile + 8, dtype=jnp.int32)[:, None]
        - jnp.arange(tile, dtype=jnp.int32)[None, :]
    )
    lag_z = (
        jnp.arange(padded.shape[2], dtype=jnp.int32)[:, None]
        - jnp.arange(out_sizes[2], dtype=jnp.int32)[None, :]
    )
    pick_y = (lag_y[None] == reach).astype(jnp.bfloat16)
    pick_z = (lag_z[None] == reach).astype(jnp.bfloat16)
    tables = jnp.einsum(
        "abc,bpy,cqz->apqyz", kernel, pick_y, pick_z, preferred_element_type=jnp.float32
    ).astype(jnp.bfloat16)
    stacked = jnp.stack([padded[offset : offset + out_sizes[0]] for offset in range(9)], axis=0)
    pieces = [
        jnp.einsum(
            "axpqm,apqyz->xyzm",
            stacked[:, :, first : first + tile + 8],
            tables,
            preferred_element_type=jnp.float32,
        )
        for first in range(0, out_sizes[1], tile)
    ]
    return jnp.concatenate(pieces, axis=1)


def gaussian_table(first_row, rows, cols, whole, gauss_width):
    row_pos = first_row + jnp.arange(rows, dtype=jnp.int32)
    col_pos = jnp.arange(cols, dtype=jnp.int32)
    spread = (row_pos[:, None] - col_pos[None, :]).astype(jnp.float32)
    width = gauss_width[:, None, None]
    table = jnp.exp(-jnp.square(spread[None] / width)) / jnp.sqrt(width)
    inside = (row_pos >= 0) & (row_pos < whole)
    return jnp.where(inside[None, :, None], table, 0.0)


def xor_gather(block, axis):
    count = lax.axis_size(axis)
    if count & (count - 1):
        return lax.all_gather(block, axis, axis=0, tiled=False), False
    parts = block[None]
    step = 1
    while step < count:
        other = lax.ppermute(parts, axis, [(i, i ^ step) for i in range(count)])
        parts = jnp.concatenate([parts, other], axis=0)
        step *= 2
    return parts, True


def gaussian_cols(first_row, rows, index, count, local, whole, gauss_width, flipped):
    row_pos = first_row + jnp.arange(rows, dtype=jnp.int32)
    place = jnp.arange(count, dtype=jnp.int32)
    source = jnp.bitwise_xor(index, place) if flipped else place
    col_pos = (source[:, None] * local + jnp.arange(local, dtype=jnp.int32)[None, :]).reshape(-1)
    spread = (row_pos[:, None] - col_pos[None, :]).astype(jnp.float32)
    width = gauss_width[:, None, None]
    table = jnp.exp(-jnp.square(spread[None] / width)) / jnp.sqrt(width)
    inside = (row_pos >= 0) & (row_pos < whole)
    return jnp.where(inside[None, :, None], table, 0.0)


def inside_mask(position, count, local, rim):
    spots = position * local - rim + jnp.arange(local + 2 * rim, dtype=jnp.int32)
    return ((spots >= 0) & (spots < local * count)).astype(jnp.float32)


def per_device(charges, kernel_fine, kernel_mid, gauss_width, gauss_weight):
    highest = lax.Precision.HIGHEST
    size_x, size_y, flat = charges.shape
    members = M
    size_z = flat // members
    field = charges.reshape(size_x, size_y, size_z, members)
    padded = padded_2(field, (("gx", 0), ("gy", 1), ("gz", 2)), 4)
    short_fine = correlate(padded, kernel_fine, (size_x, size_y, size_z), FINE_TILE)
    mid_sizes = (size_x // 2, size_y // 2, size_z // 2)
    q_mid = restrict_padded(padded, mid_sizes, 4).astype(jnp.bfloat16)
    mid_padded = padded_2(q_mid, (("gx", 0), ("gy", 1), ("gz", 2)), 6)
    short_mid = correlate(
        mid_padded, kernel_mid, (mid_sizes[0] + 4, mid_sizes[1] + 4, mid_sizes[2] + 4), MID_TILE
    )
    top_x, top_y, top_z = (size_x // 4, size_y // 4, size_z // 4)
    q_top = restrict_padded(mid_padded, (top_x, top_y, top_z), 6)
    count_x = lax.axis_size("gx")
    count_y = lax.axis_size("gy")
    count_z = lax.axis_size("gz")
    index_x = lax.axis_index("gx")
    index_y = lax.axis_index("gy")
    index_z = lax.axis_index("gz")
    whole_x = top_x * count_x
    whole_y = top_y * count_y
    whole_z = top_z * count_z
    first_x = index_x * top_x - 3
    first_y = index_y * top_y - 3
    first_z = index_z * top_z - 3
    scaled = gauss_weight[:, None, None]
    flat = q_top.reshape(-1)
    block = flat.shape[0]
    lanes = -(-block // 128) * 128
    parts = jnp.pad(flat, (0, lanes - block)).reshape(lanes // 128, 128)
    parts, flip_z = xor_gather(parts, "gz")
    parts, flip_y = xor_gather(parts, "gy")
    parts, flip_x = xor_gather(parts, "gx")
    parts = parts.reshape(count_x, count_y, count_z, lanes)[..., :block]
    parts = parts.reshape(count_x, count_y, count_z, top_x, top_y, top_z, members)
    q_full = parts.transpose(0, 3, 1, 4, 2, 5, 6).reshape(whole_x, whole_y, whole_z, members)
    table_x = gaussian_cols(first_x, top_x + 6, index_x, count_x, top_x, whole_x, gauss_width, flip_x) * scaled
    table_y = gaussian_cols(first_y, top_y + 6, index_y, count_y, top_y, whole_y, gauss_width, flip_y)
    table_z = gaussian_cols(first_z, top_z + 6, index_z, count_z, top_z, whole_z, gauss_width, flip_z)
    high = lax.Precision.HIGH
    section = jnp.einsum("gkc,abcm->gabkm", table_z, q_full, precision=high)
    section = jnp.einsum("gjb,gabkm->gajkm", table_y, section, precision=high)
    phi_top = jnp.einsum("gia,gajkm->ijkm", table_x, section, precision=high)
    ext_sizes = (mid_sizes[0] + 4, mid_sizes[1] + 4, mid_sizes[2] + 4)
    phi_mid = short_mid + prolong_ext(phi_top, ext_sizes)
    mask_x = inside_mask(index_x, count_x, mid_sizes[0], 2)
    mask_y = inside_mask(index_y, count_y, mid_sizes[1], 2)
    mask_z = inside_mask(index_z, count_z, mid_sizes[2], 2)
    phi_mid = (
        phi_mid
        * mask_x[:, None, None, None]
        * mask_y[None, :, None, None]
        * mask_z[None, None, :, None]
    )
    potential = short_fine + prolong_ext(phi_mid, (size_x, size_y, size_z))
    return potential.reshape(size_x, size_y, size_z * members)


def solution(mesh):
    placed = (P("gx", "gy", "gz"), P(), P(), P(), P())
    return jax.shard_map(
        per_device, mesh=mesh, in_specs=placed, out_specs=P("gx", "gy", "gz"), check_vma=False
    )
```
